128 devices in a mesh: lon: 8 (over x, core), lat: 16 (over y, z).
Axes of the slice: x: 4, y: 4, z: 4, core: 2. Of those that a mesh axis runs over, the one named last changes fastest.
Arguments:
- owner_tile: int32 [262144], P(('lon', 'lat')), may hold values from 0 to 127, as said below
- corner_cell: int32 [262144], P(('lon', 'lat')), may hold values from 0 to 36448
- weights: bfloat16 [4, 262144], P(None, ('lon', 'lat')), may hold values from 0.19921875 to 1
- innovations: bfloat16 [16, 262144], P(None, ('lon', 'lat')), may hold values from -6 to 6
- x_inverse: bfloat16 [2304, 2304], replicated, may hold values from 0 to 2
- y_inverse: bfloat16 [2048, 2048], replicated, may hold values from 0 to 2
Outputs:
- analysis_increment: bfloat16 [16, 2304, 2048], P(None, 'lon', 'lat')
The draws below stay inside these ranges and needn't reach their ends.
Inputs may be any that keep to these rules, and one draw needn't show every extreme that they name: `owner_tile`: among the observations of one device no tile appears more than 40 times; in every draw all 8 tiles of one latitude row appear exactly 40 times among the observations of every device.
All inputs are finite; a program needn't handle non-finite values.
Results may differ from the reference program's by a relative error of at most 0.0054.
Values may be sent and summed in bfloat16 or wider, within the bound.
No kernel may reach another device: no remote copies, remote signals or barrier semaphores. Data moves between devices by JAX's collectives and lax.ppermute only.
A program may use at most 192 MiB of HBM per device.

```python
import jax
import jax.numpy as jnp
from jax import lax

F = 4
LEV = 4
CX = 288
CY = 128
NOBS_DEV = 2048
TILES_Y = 16
NX = 2304
NY = 2048
NOBS = 262144
CAP = 40
CELLS = 36449
DEVICES = 128


def inverse_rows(key, count, reach):
    key_diag, key_left, key_right, key_rough = jax.random.split(key, 4)
    diagonal = jax.random.uniform(key_diag, (count,), jnp.float32, 0.6, 1.4)
    left_side = jax.random.uniform(key_left, (count,), jnp.float32, 0.5, 1.5)
    right_side = jax.random.uniform(key_right, (count,), jnp.float32, 0.5, 1.5)
    rough_factor = jax.random.uniform(key_rough, (count, count), jnp.float32, 0.1, 1.9)
    places = jnp.arange(count, dtype=jnp.float32)
    distance = jnp.abs(places[:, None] - places[None, :])
    coupling = 0.6 * left_side[:, None] * right_side[None, :] * jnp.exp(-distance / reach) / jnp.sqrt(reach)
    return (coupling * rough_factor + jnp.diag(diagonal)).astype(jnp.bfloat16)


def draw_x_inverse(key, part):
    reach = NX / 4.0
    return inverse_rows(jax.random.fold_in(key, 11), NX, reach)


def draw_y_inverse(key, part):
    reach = NY / 4.0
    return inverse_rows(jax.random.fold_in(key, 12), NY, reach)


def draw_innovations(key, part):
    key = jax.random.fold_in(key, 14)
    key_values = jax.random.fold_in(key, 0)
    values = jnp.clip(jax.random.normal(key_values, (F * LEV, NOBS), jnp.float32), -6.0, 6.0)
    return values.astype(jnp.bfloat16)


def draw_owner_tile(key, part):
    key = jax.random.fold_in(key, 13)
    key_hot, key_popular, key_devices = jax.random.split(key, 3)
    hot_row = jax.random.randint(key_hot, (), 0, TILES_Y)
    popular = jax.random.randint(key_popular, (DEVICES,), 0, 4)
    slot_tiles = jnp.arange(DEVICES * CAP, dtype=jnp.int32) // CAP
    base_score = jnp.where(slot_tiles % TILES_Y == hot_row, 4, popular[slot_tiles]) * 16384

    def one_device(device_key):
        key_noise, key_order = jax.random.split(device_key)
        noise = jax.random.randint(key_noise, (DEVICES * CAP,), 0, 16384)
        scores = (base_score + noise) * 16384 + jnp.arange(DEVICES * CAP, dtype=jnp.int32)
        chosen_values, chosen_slots = lax.top_k(scores, NOBS_DEV)
        chosen_tiles = chosen_slots // CAP
        return jax.random.permutation(key_order, chosen_tiles)
    device_keys = jax.random.split(key_devices, DEVICES)
    return jax.vmap(one_device)(device_keys).reshape(-1).astype(jnp.int32)


def plant(array, own_key, least, high):
    extent = array.shape
    index_at = [jax.random.randint(jax.random.fold_in(own_key, axis), (), 0, extent[axis]) for axis in range(len(extent))]
    array = array.at[tuple(index_at)].set(least)
    longest = extent.index(max(extent))
    index_at[longest] = (index_at[longest] + 1) % extent[longest]
    return array.at[tuple(index_at)].set(high)


def block_levels(stream_key, dims, cuts, low, high):
    level, own = 1.0, jax.random.fold_in(stream_key, 6)
    for axis_at, parts in cuts:
        steps = jnp.exp(jax.random.uniform(jax.random.fold_in(own, axis_at), (parts,), jnp.float32, low / len(cuts), high / len(cuts)))
        level = level * jnp.repeat(steps, dims[axis_at] // parts).reshape([-1 if axis == axis_at else 1 for axis in range(len(dims))])
    return level


def setup_inputs(seed: int = 0) -> dict:
    key_list = jax.random.split(jax.random.key(seed), 7)
    owner_tile = draw_owner_tile(jax.random.fold_in(key_list[6], 71), 0)
    corner_cell = plant(jax.random.randint(key_list[1], (NOBS,), 0, CELLS), jax.random.fold_in(key_list[1], 1), 0, CELLS - 1).astype(jnp.int32)
    weights = jnp.clip(0.19921875 + 0.80078125 * jax.random.uniform(key_list[2], (4, NOBS), jnp.float32) ** block_levels(key_list[2], (4, NOBS), ((1, 128),), -0.2, 0.2), 0.19921875, 1.0).astype(jnp.bfloat16)
    innovations = draw_innovations(jax.random.fold_in(key_list[6], 71), 0)
    x_inverse = draw_x_inverse(jax.random.fold_in(key_list[6], 71), 0)
    y_inverse = draw_y_inverse(jax.random.fold_in(key_list[6], 71), 0)
    return {"owner_tile": owner_tile, "corner_cell": corner_cell, "weights": weights, "innovations": innovations, "x_inverse": x_inverse, "y_inverse": y_inverse}


def reference(owner_tile, corner_cell, weights, innovations, x_inverse, y_inverse):
    tile_x = owner_tile // TILES_Y
    tile_y = owner_tile % TILES_Y
    base_x = tile_x * CX + corner_cell // (CY - 1)
    base_y = tile_y * CY + corner_cell % (CY - 1)
    values_wide = innovations.astype(jnp.float32)
    raw_total = jnp.zeros((F * LEV, NX * NY), jnp.float32)
    for corner in range(4):
        position = ((base_x + corner % 2) * NY + base_y + corner // 2).astype(jnp.int32)
        raw_total = raw_total.at[:, position].add(weights[corner].astype(jnp.float32)[None, :] * values_wide)
    increment = raw_total.reshape(F * LEV, NX, NY).astype(jnp.bfloat16)

    def smooth_layer(layer_field):
        along_x = jnp.dot(x_inverse, layer_field, preferred_element_type=jnp.float32).astype(jnp.bfloat16)
        return jnp.dot(along_x, y_inverse.T, preferred_element_type=jnp.float32).astype(jnp.bfloat16)

    return lax.map(smooth_layer, increment)
```

```python
import jax
import jax.numpy as jnp
from jax import lax
from jax.sharding import PartitionSpec as P


def tile_ranks(owner_tile, groups):
    obs_total = owner_tile.shape[0]
    block = 128
    blocks = obs_total // block
    one_hot = (owner_tile[:, None] == jnp.arange(groups, dtype=jnp.int32)[None, :]).astype(
        jnp.bfloat16
    )
    hot_blocks = one_hot.reshape(blocks, block, groups)
    inner = jnp.arange(block, dtype=jnp.int32)
    lower = (inner[None, :] <= inner[:, None]).astype(jnp.bfloat16)
    within = jnp.einsum("ij,bjd->bid", lower, hot_blocks, preferred_element_type=jnp.float32)
    totals = jnp.sum(hot_blocks.astype(jnp.float32), axis=1).astype(jnp.bfloat16)
    outer = jnp.arange(blocks, dtype=jnp.int32)
    before = (outer[None, :] < outer[:, None]).astype(jnp.bfloat16)
    earlier = jnp.dot(before, totals, preferred_element_type=jnp.float32)
    running = (within + earlier[:, None, :]).reshape(obs_total, groups)
    rank = jnp.sum(running * one_hot.astype(jnp.float32), axis=1).astype(jnp.int32) - 1
    return one_hot, rank


def route_obs(owner_tile, corner_cell, weights, innovations, groups, capacity, tile_cols):
    one_hot, rank = tile_ranks(owner_tile, groups)
    cell_x = corner_cell // (tile_cols - 1)
    cell_y = corner_cell % (tile_cols - 1)
    digits = jnp.stack([cell_y, cell_x % 128, cell_x // 128]).astype(jnp.bfloat16)
    stacked = jnp.concatenate([innovations, weights, digits], 0)
    rows = stacked.shape[0]
    rank_hot = rank[None, :] == jnp.arange(capacity, dtype=jnp.int32)[:, None]
    spread = jnp.where(rank_hot[None, :, :], stacked[:, None, :], jnp.zeros((), jnp.bfloat16))
    spread = spread.reshape(rows * capacity, -1)
    send = lax.dot_general(
        one_hot, spread, (((0,), (1,)), ((), ())), preferred_element_type=jnp.float32
    ).astype(jnp.bfloat16)
    got = lax.all_to_all(send, ("lon", "lat"), 0, 0, tiled=True)
    got = got.reshape(groups, rows, capacity).transpose(1, 0, 2).reshape(rows, -1)
    return got


def deposit(got, channels, tile_rows, tile_cols):
    values = got[:channels]
    got_weights = got[channels : channels + 4]
    base_y = got[channels + 4].astype(jnp.int32)
    base_x = got[channels + 5].astype(jnp.int32) + 128 * got[channels + 6].astype(jnp.int32)
    row_iota = jnp.arange(tile_rows, dtype=jnp.int32)
    col_iota = jnp.arange(tile_cols, dtype=jnp.int32)
    zero_value = jnp.zeros((), jnp.bfloat16)
    total = None
    for offset_y in range(2):
        near_rows = jnp.where(
            row_iota[:, None] == base_x[None, :], got_weights[2 * offset_y][None, :], zero_value
        )
        near_rows = near_rows + jnp.where(
            row_iota[:, None] == base_x[None, :] + 1,
            got_weights[2 * offset_y + 1][None, :],
            zero_value,
        )
        spread = jnp.where(
            col_iota[None, None, :] == (base_y + offset_y)[:, None, None],
            values.T[:, :, None],
            zero_value,
        )
        part = jnp.einsum("xo,ocy->xcy", near_rows, spread, preferred_element_type=jnp.float32)
        total = part if total is None else total + part
    return total.astype(jnp.bfloat16)


def shards(owner_tile, corner_cell, weights, innovations, x_inverse, y_inverse):
    lon_count = lax.axis_size("lon")
    lat_count = lax.axis_size("lat")
    devices = lon_count * lat_count
    channels = innovations.shape[0]
    obs_count = innovations.shape[1]
    line_x = x_inverse.shape[0]
    tile_rows = line_x // lon_count
    line_y = y_inverse.shape[0]
    tile_cols = line_y // lat_count
    capacity = 5 * obs_count // (2 * devices)
    got = route_obs(owner_tile, corner_cell, weights, innovations, devices, capacity, tile_cols)
    increment = deposit(got, channels, tile_rows, tile_cols)
    pair = channels // lon_count
    lanes = pair * tile_cols
    by_pair = increment.reshape(tile_rows, lon_count, lanes).transpose(1, 0, 2)
    lines_x = lax.all_to_all(by_pair, "lon", 0, 0, tiled=True).reshape(line_x, lanes)
    solved_x = jnp.dot(x_inverse, lines_x, preferred_element_type=jnp.float32).astype(jnp.bfloat16)
    back_x = lax.all_to_all(solved_x, "lon", 0, 1, tiled=True)
    lines_y = lax.all_to_all(back_x, "lat", 1, 1, tiled=True)
    solved_y = lax.dot_general(
        lines_y, y_inverse, (((1,), (1,)), ((), ())), preferred_element_type=jnp.float32
    ).astype(jnp.bfloat16)
    return lax.all_to_all(solved_y[None], "lat", 2, 0, tiled=True)


def solution(mesh):
    placed = (
        P(("lon", "lat")),
        P(("lon", "lat")),
        P(None, ("lon", "lat")),
        P(None, ("lon", "lat")),
        P(),
        P(),
    )
    return jax.shard_map(
        shards, mesh=mesh, in_specs=placed, out_specs=P(None, "lon", "lat"), check_vma=False
    )
```

```python
import jax
import jax.numpy as jnp
from jax import lax
from jax.sharding import PartitionSpec as P


def tile_ranks(owner_tile, groups):
    obs_total = owner_tile.shape[0]
    block = 128
    blocks = obs_total // block
    one_hot = (owner_tile[:, None] == jnp.arange(groups, dtype=jnp.int32)[None, :]).astype(
        jnp.bfloat16
    )
    hot_blocks = one_hot.reshape(blocks, block, groups)
    inner = jnp.arange(block, dtype=jnp.int32)
    lower = (inner[None, :] <= inner[:, None]).astype(jnp.bfloat16)
    within = jnp.einsum("ij,bjd->bid", lower, hot_blocks, preferred_element_type=jnp.float32)
    totals = jnp.sum(hot_blocks.astype(jnp.float32), axis=1).astype(jnp.bfloat16)
    outer = jnp.arange(blocks, dtype=jnp.int32)
    before = (outer[None, :] < outer[:, None]).astype(jnp.bfloat16)
    earlier = jnp.dot(before, totals, preferred_element_type=jnp.float32)
    running = (within + earlier[:, None, :]).reshape(obs_total, groups)
    rank = jnp.sum(running * one_hot.astype(jnp.float32), axis=1).astype(jnp.int32) - 1
    return one_hot, rank


def route_obs(owner_tile, corner_cell, weights, innovations, groups, capacity, tile_cols):
    one_hot, rank = tile_ranks(owner_tile, groups)
    cell_x = corner_cell // (tile_cols - 1)
    cell_y = corner_cell % (tile_cols - 1)
    digits = jnp.stack([cell_y, cell_x % 128, cell_x // 128]).astype(jnp.bfloat16)
    stacked = jnp.concatenate([innovations, weights, digits], 0)
    rows = stacked.shape[0]
    rank_hot = rank[None, :] == jnp.arange(capacity, dtype=jnp.int32)[:, None]
    spread = jnp.where(rank_hot[None, :, :], stacked[:, None, :], jnp.zeros((), jnp.bfloat16))
    spread = spread.reshape(rows * capacity, -1)
    send = lax.dot_general(
        one_hot, spread, (((0,), (1,)), ((), ())), preferred_element_type=jnp.float32
    ).astype(jnp.bfloat16)
    lat_count = lax.axis_size("lat")
    send = send.reshape(groups // lat_count, lat_count, rows * capacity)
    hop = lax.all_to_all(send, "lat", 1, 1, tiled=True)
    got = lax.all_to_all(hop, "lon", 0, 0, tiled=True)
    got = got.reshape(groups, rows, capacity).transpose(1, 0, 2).reshape(rows, -1)
    return got


def deposit(got, channels, tile_rows, tile_cols):
    values = got[:channels]
    got_weights = got[channels : channels + 4]
    base_y = got[channels + 4].astype(jnp.int32)
    base_x = got[channels + 5].astype(jnp.int32) + 128 * got[channels + 6].astype(jnp.int32)
    row_iota = jnp.arange(tile_rows, dtype=jnp.int32)
    col_iota = jnp.arange(tile_cols, dtype=jnp.int32)
    zero_value = jnp.zeros((), jnp.bfloat16)
    raw_total = jnp.zeros((channels, tile_rows, tile_cols), jnp.float32)
    for offset_y in range(2):
        near_rows = jnp.where(
            row_iota[None, :] == base_x[:, None], got_weights[2 * offset_y][:, None], zero_value
        )
        near_rows = near_rows + jnp.where(
            row_iota[None, :] == base_x[:, None] + 1,
            got_weights[2 * offset_y + 1][:, None],
            zero_value,
        )
        spread = jnp.where(
            col_iota[None, :, None] == (base_y + offset_y)[None, None, :],
            values[:, None, :],
            zero_value,
        )
        raw_total = raw_total + jnp.einsum(
            "cyo,ox->cxy", spread, near_rows, preferred_element_type=jnp.float32
        )
    return raw_total.astype(jnp.bfloat16)


def shards(owner_tile, corner_cell, weights, innovations, x_inverse, y_inverse):
    lon_count = lax.axis_size("lon")
    lat_count = lax.axis_size("lat")
    devices = lon_count * lat_count
    channels = innovations.shape[0]
    obs_count = innovations.shape[1]
    line_x = x_inverse.shape[0]
    tile_rows = line_x // lon_count
    line_y = y_inverse.shape[0]
    tile_cols = line_y // lat_count
    capacity = 5 * obs_count // (2 * devices)
    got = route_obs(owner_tile, corner_cell, weights, innovations, devices, capacity, tile_cols)
    increment = deposit(got, channels, tile_rows, tile_cols)
    pair = channels // lon_count
    lanes = pair * tile_cols
    by_pair = increment.reshape(lon_count, pair, tile_rows, tile_cols).transpose(0, 2, 1, 3)
    by_pair = by_pair.reshape(lon_count, tile_rows, lanes)
    lines_x = lax.all_to_all(by_pair, "lon", 0, 0, tiled=True).reshape(line_x, lanes)
    solved_x = jnp.dot(x_inverse, lines_x, preferred_element_type=jnp.float32).astype(jnp.bfloat16)
    back_x = lax.all_to_all(solved_x, "lon", 0, 1, tiled=True)
    lines_y = lax.all_to_all(back_x, "lat", 1, 1, tiled=True)
    solved_y = lax.dot_general(
        lines_y, y_inverse, (((1,), (1,)), ((), ())), preferred_element_type=jnp.float32
    ).astype(jnp.bfloat16)
    solved_y = solved_y.reshape(tile_rows, lat_count, tile_cols)
    tiles = lax.all_to_all(solved_y, "lat", 1, 1, tiled=True)
    return tiles.transpose(1, 0, 2)


def solution(mesh):
    placed = (
        P(("lon", "lat")),
        P(("lon", "lat")),
        P(None, ("lon", "lat")),
        P(None, ("lon", "lat")),
        P(),
        P(),
    )
    return jax.shard_map(
        shards, mesh=mesh, in_specs=placed, out_specs=P(None, "lon", "lat"), check_vma=False
    )
```

```python
import jax
import jax.numpy as jnp
from jax import lax
from jax.sharding import PartitionSpec as P


def tile_ranks(owner_tile, groups):
    obs_total = owner_tile.shape[0]
    block = 128
    blocks = obs_total // block
    one_hot = (owner_tile[:, None] == jnp.arange(groups, dtype=jnp.int32)[None, :]).astype(
        jnp.bfloat16
    )
    hot_blocks = one_hot.reshape(blocks, block, groups)
    inner = jnp.arange(block, dtype=jnp.int32)
    lower = (inner[None, :] <= inner[:, None]).astype(jnp.bfloat16)
    within = jnp.einsum("ij,bjd->bid", lower, hot_blocks, preferred_element_type=jnp.float32)
    totals = jnp.sum(hot_blocks.astype(jnp.float32), axis=1).astype(jnp.bfloat16)
    outer = jnp.arange(blocks, dtype=jnp.int32)
    before = (outer[None, :] < outer[:, None]).astype(jnp.bfloat16)
    earlier = jnp.dot(before, totals, preferred_element_type=jnp.float32)
    running = (within + earlier[:, None, :]).reshape(obs_total, groups)
    rank = jnp.sum(running * one_hot.astype(jnp.float32), axis=1).astype(jnp.int32) - 1
    return one_hot, rank


def route_obs(owner_tile, corner_cell, weights, innovations, capacity, tile_cols):
    lon_count = lax.axis_size("lon")
    lat_count = lax.axis_size("lat")
    groups = lon_count * lat_count
    channels = innovations.shape[0]
    pair = channels // lon_count
    one_hot, rank = tile_ranks(owner_tile, groups)
    cell_x = corner_cell // (tile_cols - 1)
    cell_y = corner_cell % (tile_cols - 1)
    digits = jnp.stack([cell_y, cell_x % 128, cell_x // 128]).astype(jnp.bfloat16)
    stacked = jnp.concatenate([innovations, weights, digits], 0)
    rows = stacked.shape[0]
    rank_hot = rank[None, :] == jnp.arange(capacity, dtype=jnp.int32)[:, None]
    spread = jnp.where(rank_hot[None, :, :], stacked[:, None, :], jnp.zeros((), jnp.bfloat16))
    spread = spread.reshape(rows * capacity, -1)
    placed = lax.dot_general(
        one_hot, spread, (((0,), (1,)), ((), ())), preferred_element_type=jnp.float32
    ).astype(jnp.bfloat16)
    placed = placed.reshape(lon_count, lat_count, rows, capacity)
    shared = rows - channels
    by_pair = placed[:, :, :channels].reshape(lon_count, lat_count, lon_count, pair, capacity)
    common = jnp.broadcast_to(
        placed[:, :, None, channels:], (lon_count, lat_count, lon_count, shared, capacity)
    )
    send = jnp.concatenate([by_pair, common], 3).transpose(2, 1, 0, 3, 4)
    send = send.reshape(groups, -1)
    got = lax.all_to_all(send, ("lon", "lat"), 0, 0, tiled=True)
    got = got.reshape(groups, lon_count, pair + shared, capacity).transpose(1, 2, 0, 3)
    return got.reshape(lon_count, pair + shared, groups * capacity)


def deposit(got, pair, tile_rows, tile_cols):
    values = got[:, :pair]
    got_weights = got[:, pair : pair + 4]
    base_y = got[:, pair + 4].astype(jnp.int32)
    base_x = got[:, pair + 5].astype(jnp.int32) + 128 * got[:, pair + 6].astype(jnp.int32)
    row_iota = jnp.arange(tile_rows, dtype=jnp.int32)
    col_iota = jnp.arange(tile_cols, dtype=jnp.int32)
    zero_value = jnp.zeros((), jnp.bfloat16)
    raw_total = None
    for offset_y in range(2):
        near_rows = jnp.where(
            row_iota[None, :, None] == base_x[:, None, :],
            got_weights[:, 2 * offset_y][:, None, :],
            zero_value,
        )
        near_rows = near_rows + jnp.where(
            row_iota[None, :, None] == base_x[:, None, :] + 1,
            got_weights[:, 2 * offset_y + 1][:, None, :],
            zero_value,
        )
        spread = jnp.where(
            col_iota[None, None, :, None] == (base_y + offset_y)[:, None, None, :],
            values[:, :, None, :],
            zero_value,
        )
        spread = spread.reshape(spread.shape[0], pair * tile_cols, -1)
        part = jnp.einsum("txo,tco->txc", near_rows, spread, preferred_element_type=jnp.float32)
        raw_total = part if raw_total is None else raw_total + part
    return raw_total.astype(jnp.bfloat16)


def shards(owner_tile, corner_cell, weights, innovations, x_inverse, y_inverse):
    lon_count = lax.axis_size("lon")
    lat_count = lax.axis_size("lat")
    devices = lon_count * lat_count
    channels = innovations.shape[0]
    obs_count = innovations.shape[1]
    line_x = x_inverse.shape[0]
    tile_rows = line_x // lon_count
    line_y = y_inverse.shape[0]
    tile_cols = line_y // lat_count
    capacity = 5 * obs_count // (2 * devices)
    pair = channels // lon_count
    lanes = pair * tile_cols
    got = route_obs(owner_tile, corner_cell, weights, innovations, capacity, tile_cols)
    lines_x = deposit(got, pair, tile_rows, tile_cols).reshape(line_x, lanes)
    solved_x = jnp.dot(x_inverse, lines_x, preferred_element_type=jnp.float32).astype(jnp.bfloat16)
    back_x = lax.all_to_all(solved_x, "lon", 0, 1, tiled=True)
    lines_y = lax.all_to_all(back_x, "lat", 1, 1, tiled=True)
    solved_y = lax.dot_general(
        lines_y, y_inverse, (((1,), (1,)), ((), ())), preferred_element_type=jnp.float32
    ).astype(jnp.bfloat16)
    solved_y = solved_y.reshape(tile_rows, lat_count, tile_cols)
    tiles = lax.all_to_all(solved_y, "lat", 1, 1, tiled=True)
    return tiles.transpose(1, 0, 2)


def solution(mesh):
    placed = (
        P(("lon", "lat")),
        P(("lon", "lat")),
        P(None, ("lon", "lat")),
        P(None, ("lon", "lat")),
        P(),
        P(),
    )
    return jax.shard_map(
        shards, mesh=mesh, in_specs=placed, out_specs=P(None, "lon", "lat"), check_vma=False
    )
```

```python
import jax
import jax.numpy as jnp
from jax import lax
from jax.sharding import PartitionSpec as P


def tile_ranks(owner_tile, groups):
    obs_total = owner_tile.shape[0]
    block = 128
    blocks = obs_total // block
    one_hot = (owner_tile[:, None] == jnp.arange(groups, dtype=jnp.int32)[None, :]).astype(
        jnp.bfloat16
    )
    hot_blocks = one_hot.reshape(blocks, block, groups)
    inner = jnp.arange(block, dtype=jnp.int32)
    lower = (inner[None, :] <= inner[:, None]).astype(jnp.bfloat16)
    within = jnp.einsum("ij,bjd->bid", lower, hot_blocks, preferred_element_type=jnp.float32)
    totals = jnp.sum(hot_blocks.astype(jnp.float32), axis=1).astype(jnp.bfloat16)
    outer = jnp.arange(blocks, dtype=jnp.int32)
    before = (outer[None, :] < outer[:, None]).astype(jnp.bfloat16)
    earlier = jnp.dot(before, totals, preferred_element_type=jnp.float32)
    running = (within + earlier[:, None, :]).reshape(obs_total, groups)
    rank = jnp.sum(running * one_hot.astype(jnp.float32), axis=1).astype(jnp.int32) - 1
    return one_hot, rank


def route_obs(owner_tile, corner_cell, weights, innovations, groups, capacity, tile_cols):
    one_hot, rank = tile_ranks(owner_tile, groups)
    cell_x = corner_cell // (tile_cols - 1)
    cell_y = corner_cell % (tile_cols - 1)
    digits = jnp.stack([cell_y, cell_x % 128, cell_x // 128]).astype(jnp.bfloat16)
    stacked = jnp.concatenate([innovations, weights, digits], 0)
    rows = stacked.shape[0]
    rank_hot = rank[None, :] == jnp.arange(capacity, dtype=jnp.int32)[:, None]
    spread = jnp.where(rank_hot[None, :, :], stacked[:, None, :], jnp.zeros((), jnp.bfloat16))
    spread = spread.reshape(rows * capacity, -1)
    send = lax.dot_general(
        one_hot, spread, (((0,), (1,)), ((), ())), preferred_element_type=jnp.float32
    ).astype(jnp.bfloat16)
    got = lax.all_to_all(send, ("lon", "lat"), 0, 0, tiled=True)
    got = got.reshape(groups, rows, capacity).transpose(1, 0, 2).reshape(rows, -1)
    return got


def deposit(got, channels, tile_rows, tile_cols):
    values = got[:channels]
    got_weights = got[channels : channels + 4]
    base_y = got[channels + 4].astype(jnp.int32)
    base_x = got[channels + 5].astype(jnp.int32) + 128 * got[channels + 6].astype(jnp.int32)
    row_iota = jnp.arange(tile_rows, dtype=jnp.int32)
    col_iota = jnp.arange(tile_cols, dtype=jnp.int32)
    zero_value = jnp.zeros((), jnp.bfloat16)
    raw_total = jnp.zeros((channels, tile_rows, tile_cols), jnp.float32)
    for offset_y in range(2):
        near_rows = jnp.where(
            row_iota[None, :] == base_x[:, None], got_weights[2 * offset_y][:, None], zero_value
        )
        near_rows = near_rows + jnp.where(
            row_iota[None, :] == base_x[:, None] + 1,
            got_weights[2 * offset_y + 1][:, None],
            zero_value,
        )
        spread = jnp.where(
            col_iota[None, :, None] == (base_y + offset_y)[None, None, :],
            values[:, None, :],
            zero_value,
        )
        raw_total = raw_total + jnp.einsum(
            "cyo,ox->cxy", spread, near_rows, preferred_element_type=jnp.float32
        )
    return raw_total.astype(jnp.bfloat16)


def shards(owner_tile, corner_cell, weights, innovations, x_inverse, y_inverse):
    lon_count = lax.axis_size("lon")
    lat_count = lax.axis_size("lat")
    devices = lon_count * lat_count
    channels = innovations.shape[0]
    obs_count = innovations.shape[1]
    line_x = x_inverse.shape[0]
    tile_rows = line_x // lon_count
    line_y = y_inverse.shape[0]
    tile_cols = line_y // lat_count
    capacity = 5 * obs_count // (2 * devices)
    got = route_obs(owner_tile, corner_cell, weights, innovations, devices, capacity, tile_cols)
    increment = deposit(got, channels, tile_rows, tile_cols)
    pair = channels // lon_count
    lanes = pair * tile_cols
    by_pair = increment.reshape(lon_count, pair, tile_rows, tile_cols).transpose(0, 2, 1, 3)
    by_pair = by_pair.reshape(lon_count, tile_rows, lanes)
    lines_x = lax.all_to_all(by_pair, "lon", 0, 0, tiled=True).reshape(line_x, lanes)
    solved_x = jnp.dot(x_inverse, lines_x, preferred_element_type=jnp.float32).astype(jnp.bfloat16)
    stride = tile_rows // lat_count
    by_row = solved_x.reshape(lon_count, stride, lat_count, lanes).transpose(0, 2, 1, 3)
    by_row = by_row.reshape(devices, stride, lanes)
    got = lax.all_to_all(by_row, ("lon", "lat"), 0, 0, tiled=True)
    got = got.reshape(lon_count, lat_count, stride, pair, tile_cols).transpose(0, 3, 2, 1, 4)
    lines_y = got.reshape(channels * stride, line_y)
    solved_y = lax.dot_general(
        lines_y, y_inverse, (((1,), (1,)), ((), ())), preferred_element_type=jnp.float32
    ).astype(jnp.bfloat16)
    solved_y = solved_y.reshape(channels * stride, lat_count, tile_cols)
    tiles = lax.all_to_all(solved_y, "lat", 1, 1, tiled=True)
    return tiles.reshape(channels, tile_rows, tile_cols)


def solution(mesh):
    placed = (
        P(("lon", "lat")),
        P(("lon", "lat")),
        P(None, ("lon", "lat")),
        P(None, ("lon", "lat")),
        P(),
        P(),
    )
    return jax.shard_map(
        shards, mesh=mesh, in_specs=placed, out_specs=P(None, "lon", "lat"), check_vma=False
    )
```

```python
import jax
import jax.numpy as jnp
from jax import lax
from jax.sharding import PartitionSpec as P


def tile_ranks(owner_tile, groups):
    obs_total = owner_tile.shape[0]
    block = 128
    blocks = obs_total // block
    one_hot = (owner_tile[:, None] == jnp.arange(groups, dtype=jnp.int32)[None, :]).astype(
        jnp.bfloat16
    )
    hot_blocks = one_hot.reshape(blocks, block, groups)
    inner = jnp.arange(block, dtype=jnp.int32)
    lower = (inner[None, :] <= inner[:, None]).astype(jnp.bfloat16)
    within = jnp.einsum("ij,bjd->bid", lower, hot_blocks, preferred_element_type=jnp.float32)
    totals = jnp.sum(hot_blocks.astype(jnp.float32), axis=1).astype(jnp.bfloat16)
    outer = jnp.arange(blocks, dtype=jnp.int32)
    before = (outer[None, :] < outer[:, None]).astype(jnp.bfloat16)
    earlier = jnp.dot(before, totals, preferred_element_type=jnp.float32)
    running = (within + earlier[:, None, :]).reshape(obs_total, groups)
    rank = jnp.sum(running * one_hot.astype(jnp.float32), axis=1).astype(jnp.int32) - 1
    return one_hot, rank


def route_obs(owner_tile, corner_cell, weights, innovations, groups, capacity, tile_cols):
    one_hot, rank = tile_ranks(owner_tile, groups)
    cell_x = corner_cell // (tile_cols - 1)
    cell_y = corner_cell % (tile_cols - 1)
    digits = jnp.stack([cell_y, cell_x % 128, cell_x // 128]).astype(jnp.bfloat16)
    stacked = jnp.concatenate([innovations, weights, digits], 0)
    rows = stacked.shape[0]
    rank_hot = rank[None, :] == jnp.arange(capacity, dtype=jnp.int32)[:, None]
    spread = jnp.where(rank_hot[None, :, :], stacked[:, None, :], jnp.zeros((), jnp.bfloat16))
    spread = spread.reshape(rows * capacity, -1)
    send = lax.dot_general(
        one_hot, spread, (((0,), (1,)), ((), ())), preferred_element_type=jnp.float32
    ).astype(jnp.bfloat16)
    got = lax.all_to_all(send, ("lon", "lat"), 0, 0, tiled=True)
    got = got.reshape(groups, rows, capacity).transpose(1, 0, 2).reshape(rows, -1)
    return got


def deposit(got, channels, tile_rows, tile_cols):
    values = got[:channels]
    got_weights = got[channels : channels + 4]
    base_y = got[channels + 4].astype(jnp.int32)
    base_x = got[channels + 5].astype(jnp.int32) + 128 * got[channels + 6].astype(jnp.int32)
    row_iota = jnp.arange(tile_rows, dtype=jnp.int32)
    col_iota = jnp.arange(tile_cols, dtype=jnp.int32)
    zero_value = jnp.zeros((), jnp.bfloat16)
    near = []
    for offset_y in range(2):
        near_rows = jnp.where(
            row_iota[None, :] == base_x[:, None], got_weights[2 * offset_y][:, None], zero_value
        )
        near_rows = near_rows + jnp.where(
            row_iota[None, :] == base_x[:, None] + 1,
            got_weights[2 * offset_y + 1][:, None],
            zero_value,
        )
        near.append(near_rows)
    near = jnp.stack(near, 1)
    spread = jnp.where(
        col_iota[None, :, None] == base_y[None, None, :], values[:, None, :], zero_value
    )
    both = jnp.einsum("cyo,odx->dcxy", spread, near, preferred_element_type=jnp.float32)
    shifted = jnp.pad(both[1, :, :, :-1], ((0, 0), (0, 0), (1, 0)))
    return (both[0] + shifted).astype(jnp.bfloat16)


def shards(owner_tile, corner_cell, weights, innovations, x_inverse, y_inverse):
    lon_count = lax.axis_size("lon")
    lat_count = lax.axis_size("lat")
    devices = lon_count * lat_count
    channels = innovations.shape[0]
    obs_count = innovations.shape[1]
    line_x = x_inverse.shape[0]
    tile_rows = line_x // lon_count
    line_y = y_inverse.shape[0]
    tile_cols = line_y // lat_count
    capacity = 5 * obs_count // (2 * devices)
    got = route_obs(owner_tile, corner_cell, weights, innovations, devices, capacity, tile_cols)
    increment = deposit(got, channels, tile_rows, tile_cols)
    pair = channels // lon_count
    lanes = pair * tile_cols
    by_pair = increment.reshape(lon_count, pair, tile_rows, tile_cols).transpose(0, 2, 1, 3)
    by_pair = by_pair.reshape(lon_count, tile_rows, lanes)
    lines_x = lax.all_to_all(by_pair, "lon", 0, 0, tiled=True).reshape(line_x, lanes)
    solved_x = jnp.dot(x_inverse, lines_x, preferred_element_type=jnp.float32).astype(jnp.bfloat16)
    stride = tile_rows // lat_count
    by_row = solved_x.reshape(lon_count, stride, lat_count, lanes).transpose(0, 2, 1, 3)
    by_row = by_row.reshape(devices, stride, lanes)
    got = lax.all_to_all(by_row, ("lon", "lat"), 0, 0, tiled=True)
    got = got.reshape(lon_count, lat_count, stride, pair, tile_cols).transpose(0, 3, 2, 1, 4)
    lines_y = got.reshape(channels * stride, line_y)
    solved_y = lax.dot_general(
        lines_y, y_inverse, (((1,), (1,)), ((), ())), preferred_element_type=jnp.float32
    ).astype(jnp.bfloat16)
    solved_y = solved_y.reshape(channels * stride, lat_count, tile_cols)
    tiles = lax.all_to_all(solved_y, "lat", 1, 1, tiled=True)
    return tiles.reshape(channels, tile_rows, tile_cols)


def solution(mesh):
    placed = (
        P(("lon", "lat")),
        P(("lon", "lat")),
        P(None, ("lon", "lat")),
        P(None, ("lon", "lat")),
        P(),
        P(),
    )
    return jax.shard_map(
        shards, mesh=mesh, in_specs=placed, out_specs=P(None, "lon", "lat"), check_vma=False
    )
```

```python
import jax
import jax.numpy as jnp
from jax import lax
from jax.sharding import PartitionSpec as P


def tile_ranks(owner_tile, groups):
    obs_total = owner_tile.shape[0]
    block = 128
    blocks = obs_total // block
    one_hot = (owner_tile[:, None] == jnp.arange(groups, dtype=jnp.int32)[None, :]).astype(
        jnp.bfloat16
    )
    hot_blocks = one_hot.reshape(blocks, block, groups)
    inner = jnp.arange(block, dtype=jnp.int32)
    lower = (inner[None, :] <= inner[:, None]).astype(jnp.bfloat16)
    within = jnp.einsum("ij,bjd->bid", lower, hot_blocks, preferred_element_type=jnp.float32)
    totals = jnp.sum(hot_blocks.astype(jnp.float32), axis=1).astype(jnp.bfloat16)
    outer = jnp.arange(blocks, dtype=jnp.int32)
    before = (outer[None, :] < outer[:, None]).astype(jnp.bfloat16)
    earlier = jnp.dot(before, totals, preferred_element_type=jnp.float32)
    running = (within + earlier[:, None, :]).reshape(obs_total, groups)
    rank = jnp.sum(running * one_hot.astype(jnp.float32), axis=1).astype(jnp.int32) - 1
    return one_hot, rank


def route_obs(owner_tile, corner_cell, weights, innovations, capacity, tile_cols):
    lon_count = lax.axis_size("lon")
    lat_count = lax.axis_size("lat")
    groups = lon_count * lat_count
    channels = innovations.shape[0]
    pair = channels // lon_count
    one_hot, rank = tile_ranks(owner_tile, groups)
    cell_x = corner_cell // (tile_cols - 1)
    cell_y = corner_cell % (tile_cols - 1)
    digits = jnp.stack([cell_y, cell_x % 128, cell_x // 128]).astype(jnp.bfloat16)
    stacked = jnp.concatenate([innovations, weights, digits], 0)
    rows = stacked.shape[0]
    shared = rows - channels
    rank_hot = rank[None, :] == jnp.arange(capacity, dtype=jnp.int32)[:, None]
    spread = jnp.where(rank_hot[None, :, :], stacked[:, None, :], jnp.zeros((), jnp.bfloat16))
    spread = spread.reshape(rows * capacity, -1)
    placed = lax.dot_general(
        one_hot, spread, (((0,), (1,)), ((), ())), preferred_element_type=jnp.float32
    ).astype(jnp.bfloat16)
    placed = placed.reshape(lon_count, lat_count, rows, capacity)
    by_pair = placed[:, :, :channels].reshape(lon_count, lat_count, lon_count, pair, capacity)
    by_pair = by_pair.transpose(2, 1, 3, 0, 4).reshape(lon_count, lat_count, -1)
    common = placed[:, :, channels:].transpose(1, 2, 0, 3).reshape(lat_count, -1)
    common = jnp.broadcast_to(common[None], (lon_count,) + common.shape)
    send = jnp.concatenate([by_pair, common], 2).reshape(groups, -1)
    got = lax.all_to_all(send, ("lon", "lat"), 0, 0, tiled=True)
    got = got.reshape(groups, pair + shared, lon_count, capacity).transpose(2, 1, 0, 3)
    return got.reshape(lon_count, pair + shared, groups * capacity)


def deposit(got, pair, tile_rows, tile_cols):
    values = got[:, :pair]
    got_weights = got[:, pair : pair + 4]
    base_y = got[:, pair + 4].astype(jnp.int32)
    base_x = got[:, pair + 5].astype(jnp.int32) + 128 * got[:, pair + 6].astype(jnp.int32)
    row_iota = jnp.arange(tile_rows, dtype=jnp.int32)
    col_iota = jnp.arange(tile_cols, dtype=jnp.int32)
    zero_value = jnp.zeros((), jnp.bfloat16)
    raw_total = None
    for offset_y in range(2):
        near_rows = jnp.where(
            row_iota[None, None, :] == base_x[:, :, None],
            got_weights[:, 2 * offset_y][:, :, None],
            zero_value,
        )
        near_rows = near_rows + jnp.where(
            row_iota[None, None, :] == base_x[:, :, None] + 1,
            got_weights[:, 2 * offset_y + 1][:, :, None],
            zero_value,
        )
        spread = jnp.where(
            col_iota[None, None, :, None] == (base_y + offset_y)[:, None, None, :],
            values[:, :, None, :],
            zero_value,
        )
        part = jnp.einsum("tcyo,tox->tcxy", spread, near_rows, preferred_element_type=jnp.float32)
        raw_total = part if raw_total is None else raw_total + part
    return raw_total.astype(jnp.bfloat16)


def shards(owner_tile, corner_cell, weights, innovations, x_inverse, y_inverse):
    lon_count = lax.axis_size("lon")
    lat_count = lax.axis_size("lat")
    devices = lon_count * lat_count
    channels = innovations.shape[0]
    obs_count = innovations.shape[1]
    line_x = x_inverse.shape[0]
    tile_rows = line_x // lon_count
    line_y = y_inverse.shape[0]
    tile_cols = line_y // lat_count
    capacity = 5 * obs_count // (2 * devices)
    pair = channels // lon_count
    lanes = pair * tile_cols
    got = route_obs(owner_tile, corner_cell, weights, innovations, capacity, tile_cols)
    increment = deposit(got, pair, tile_rows, tile_cols)
    lines_x = increment.transpose(0, 2, 1, 3).reshape(line_x, lanes)
    solved_x = jnp.dot(x_inverse, lines_x, preferred_element_type=jnp.float32).astype(jnp.bfloat16)
    stride = tile_rows // lat_count
    by_row = solved_x.reshape(lon_count, stride, lat_count, lanes).transpose(0, 2, 1, 3)
    by_row = by_row.reshape(devices, stride, lanes)
    got = lax.all_to_all(by_row, ("lon", "lat"), 0, 0, tiled=True)
    got = got.reshape(lon_count, lat_count, stride, pair, tile_cols).transpose(0, 3, 2, 1, 4)
    lines_y = got.reshape(channels * stride, line_y)
    solved_y = lax.dot_general(
        lines_y, y_inverse, (((1,), (1,)), ((), ())), preferred_element_type=jnp.float32
    ).astype(jnp.bfloat16)
    solved_y = solved_y.reshape(channels * stride, lat_count, tile_cols)
    tiles = lax.all_to_all(solved_y, "lat", 1, 1, tiled=True)
    return tiles.reshape(channels, tile_rows, tile_cols)


def solution(mesh):
    placed = (
        P(("lon", "lat")),
        P(("lon", "lat")),
        P(None, ("lon", "lat")),
        P(None, ("lon", "lat")),
        P(),
        P(),
    )
    return jax.shard_map(
        shards, mesh=mesh, in_specs=placed, out_specs=P(None, "lon", "lat"), check_vma=False
    )
```

```python
import jax
import jax.numpy as jnp
from jax import lax
from jax.sharding import PartitionSpec as P


def tile_ranks(owner_tile, groups):
    obs_total = owner_tile.shape[0]
    block = 128
    blocks = obs_total // block
    one_hot = (owner_tile[:, None] == jnp.arange(groups, dtype=jnp.int32)[None, :]).astype(
        jnp.bfloat16
    )
    hot_blocks = one_hot.reshape(blocks, block, groups)
    inner = jnp.arange(block, dtype=jnp.int32)
    lower = (inner[None, :] <= inner[:, None]).astype(jnp.bfloat16)
    within = jnp.einsum("ij,bjd->bid", lower, hot_blocks, preferred_element_type=jnp.float32)
    totals = jnp.sum(hot_blocks.astype(jnp.float32), axis=1).astype(jnp.bfloat16)
    outer = jnp.arange(blocks, dtype=jnp.int32)
    before = (outer[None, :] < outer[:, None]).astype(jnp.bfloat16)
    earlier = jnp.dot(before, totals, preferred_element_type=jnp.float32)
    running = (within + earlier[:, None, :]).reshape(obs_total, groups)
    rank = jnp.sum(running * one_hot.astype(jnp.float32), axis=1).astype(jnp.int32) - 1
    return one_hot, rank


def route_obs(owner_tile, corner_cell, weights, innovations, groups, capacity, tile_cols):
    one_hot, rank = tile_ranks(owner_tile, groups)
    cell_x = corner_cell // (tile_cols - 1)
    cell_y = corner_cell % (tile_cols - 1)
    digits = jnp.stack([cell_y, cell_x % 128, cell_x // 128]).astype(jnp.bfloat16)
    stacked = jnp.concatenate([innovations, weights, digits], 0)
    rows = stacked.shape[0]
    rank_hot = rank[None, :] == jnp.arange(capacity, dtype=jnp.int32)[:, None]
    spread = jnp.where(rank_hot[None, :, :], stacked[:, None, :], jnp.zeros((), jnp.bfloat16))
    spread = spread.reshape(rows * capacity, -1)
    send = lax.dot_general(
        one_hot, spread, (((0,), (1,)), ((), ())), preferred_element_type=jnp.float32
    ).astype(jnp.bfloat16)
    got = lax.all_to_all(send, ("lon", "lat"), 0, 0, tiled=True)
    got = got.reshape(groups, rows, capacity).transpose(1, 0, 2).reshape(rows, -1)
    return got


def deposit(got, channels, tile_rows, tile_cols):
    values = got[:channels]
    got_weights = got[channels : channels + 4]
    base_y = got[channels + 4].astype(jnp.int32)
    base_x = got[channels + 5].astype(jnp.int32) + 128 * got[channels + 6].astype(jnp.int32)
    row_iota = jnp.arange(tile_rows, dtype=jnp.int32)
    col_iota = jnp.arange(tile_cols, dtype=jnp.int32)
    zero_value = jnp.zeros((), jnp.bfloat16)
    raw_total = jnp.zeros((channels, tile_rows, tile_cols), jnp.float32)
    for offset_y in range(2):
        near_rows = jnp.where(
            row_iota[None, :] == base_x[:, None], got_weights[2 * offset_y][:, None], zero_value
        )
        near_rows = near_rows + jnp.where(
            row_iota[None, :] == base_x[:, None] + 1,
            got_weights[2 * offset_y + 1][:, None],
            zero_value,
        )
        spread = jnp.where(
            col_iota[None, :, None] == (base_y + offset_y)[None, None, :],
            values[:, None, :],
            zero_value,
        )
        raw_total = raw_total + jnp.einsum(
            "cyo,ox->cxy", spread, near_rows, preferred_element_type=jnp.float32
        )
    return raw_total.astype(jnp.bfloat16)


def shards(owner_tile, corner_cell, weights, innovations, x_inverse, y_inverse):
    lon_count = lax.axis_size("lon")
    lat_count = lax.axis_size("lat")
    devices = lon_count * lat_count
    channels = innovations.shape[0]
    obs_count = innovations.shape[1]
    line_x = x_inverse.shape[0]
    tile_rows = line_x // lon_count
    line_y = y_inverse.shape[0]
    tile_cols = line_y // lat_count
    capacity = 5 * obs_count // (2 * devices)
    got = route_obs(owner_tile, corner_cell, weights, innovations, devices, capacity, tile_cols)
    increment = deposit(got, channels, tile_rows, tile_cols)
    pair = channels // lon_count
    lanes = pair * tile_cols
    lines_x = lax.all_to_all(increment, "lon", 0, 0, tiled=True)
    lines_x = lines_x.reshape(lon_count, pair, tile_rows, tile_cols)
    x_blocks = x_inverse.reshape(line_x, lon_count, tile_rows)
    solved_x = lax.dot_general(
        x_blocks, lines_x, (((1, 2), (0, 2)), ((), ())), preferred_element_type=jnp.float32
    )
    solved_x = solved_x.astype(jnp.bfloat16).reshape(line_x, lanes)
    stride = tile_rows // lat_count
    by_row = solved_x.reshape(lon_count, stride, lat_count, lanes).transpose(0, 2, 1, 3)
    by_row = by_row.reshape(devices, stride, lanes)
    got = lax.all_to_all(by_row, ("lon", "lat"), 0, 0, tiled=True)
    got = got.reshape(lon_count, lat_count, stride, pair, tile_cols).transpose(0, 3, 2, 1, 4)
    lines_y = got.reshape(channels * stride, line_y)
    solved_y = lax.dot_general(
        lines_y, y_inverse, (((1,), (1,)), ((), ())), preferred_element_type=jnp.float32
    ).astype(jnp.bfloat16)
    solved_y = solved_y.reshape(channels * stride, lat_count, tile_cols)
    tiles = lax.all_to_all(solved_y, "lat", 1, 1, tiled=True)
    return tiles.reshape(channels, tile_rows, tile_cols)


def solution(mesh):
    placed = (
        P(("lon", "lat")),
        P(("lon", "lat")),
        P(None, ("lon", "lat")),
        P(None, ("lon", "lat")),
        P(),
        P(),
    )
    return jax.shard_map(
        shards, mesh=mesh, in_specs=placed, out_specs=P(None, "lon", "lat"), check_vma=False
    )
```

```python
import jax
import jax.numpy as jnp
from jax import lax
from jax.sharding import PartitionSpec as P
from jax.experimental import pallas as pl
from jax.experimental.pallas import tpu as pltpu


def tile_ranks(owner_tile, groups):
    obs_total = owner_tile.shape[0]
    block = 128
    blocks = obs_total // block
    one_hot = (owner_tile[:, None] == jnp.arange(groups, dtype=jnp.int32)[None, :]).astype(
        jnp.bfloat16
    )
    hot_blocks = one_hot.reshape(blocks, block, groups)
    inner = jnp.arange(block, dtype=jnp.int32)
    lower = (inner[None, :] <= inner[:, None]).astype(jnp.bfloat16)
    within = jnp.einsum("ij,bjd->bid", lower, hot_blocks, preferred_element_type=jnp.float32)
    totals = jnp.sum(hot_blocks.astype(jnp.float32), axis=1).astype(jnp.bfloat16)
    outer = jnp.arange(blocks, dtype=jnp.int32)
    before = (outer[None, :] < outer[:, None]).astype(jnp.bfloat16)
    earlier = jnp.dot(before, totals, preferred_element_type=jnp.float32)
    running = (within + earlier[:, None, :]).reshape(obs_total, groups)
    rank = jnp.sum(running * one_hot.astype(jnp.float32), axis=1).astype(jnp.int32) - 1
    return one_hot, rank


def route_obs(owner_tile, corner_cell, weights, innovations, groups, capacity, tile_cols):
    one_hot, rank = tile_ranks(owner_tile, groups)
    cell_x = corner_cell // (tile_cols - 1)
    cell_y = corner_cell % (tile_cols - 1)
    digits = jnp.stack([cell_y, cell_x % 128, cell_x // 128]).astype(jnp.bfloat16)
    stacked = jnp.concatenate([innovations, weights, digits], 0)
    rows = stacked.shape[0]
    rank_hot = rank[None, :] == jnp.arange(capacity, dtype=jnp.int32)[:, None]
    spread = jnp.where(rank_hot[None, :, :], stacked[:, None, :], jnp.zeros((), jnp.bfloat16))
    spread = spread.reshape(rows * capacity, -1)
    send = lax.dot_general(
        one_hot, spread, (((0,), (1,)), ((), ())), preferred_element_type=jnp.float32
    ).astype(jnp.bfloat16)
    got = lax.all_to_all(send, ("lon", "lat"), 0, 0, tiled=True)
    got = got.reshape(groups, rows, capacity).transpose(1, 0, 2).reshape(rows, -1)
    return got


def deposit_kernel(vals_ref, by_ref, bx_ref, w_ref, out_ref, acc_ref, spread_ref):
    step = pl.program_id(0)
    chunk, channels = vals_ref.shape
    tile_rows = out_ref.shape[0]
    tile_cols = out_ref.shape[1] // channels

    @pl.when(step == 0)
    def _():
        acc_ref[...] = jnp.zeros_like(acc_ref)

    zero = jnp.zeros((), jnp.bfloat16)
    lane_y = lax.broadcasted_iota(jnp.int32, (chunk, tile_cols), 1)
    hit_y = lane_y == by_ref[...]
    for c in range(channels):
        spread_ref[:, c * tile_cols : (c + 1) * tile_cols] = jnp.where(
            hit_y, vals_ref[:, c : c + 1], zero
        )
    row_x = lax.broadcasted_iota(jnp.int32, (tile_rows, chunk), 0)
    base_x = bx_ref[...]
    at_x = row_x == base_x
    next_x = row_x == base_x + 1
    for offset_y in range(2):
        near = jnp.where(at_x, w_ref[2 * offset_y : 2 * offset_y + 1, :], zero) + jnp.where(
            next_x, w_ref[2 * offset_y + 1 : 2 * offset_y + 2, :], zero
        )
        acc_ref[offset_y] += jnp.dot(near, spread_ref[...], preferred_element_type=jnp.float32)

    @pl.when(step == pl.num_programs(0) - 1)
    def _():
        later = pltpu.roll(acc_ref[1], 1, 1)
        lane = lax.broadcasted_iota(jnp.int32, later.shape, 1)
        later = jnp.where(lane % tile_cols == 0, 0.0, later)
        out_ref[...] = (acc_ref[0] + later).astype(out_ref.dtype)


def deposit(got, channels, tile_rows, tile_cols):
    obs = got.shape[1]
    chunk = 512
    vals_col = got[:channels].T
    by_col = got[channels + 4].astype(jnp.int32)[:, None]
    bx_row = (got[channels + 5].astype(jnp.int32) + 128 * got[channels + 6].astype(jnp.int32))[None, :]
    w_row = got[channels : channels + 4]
    lanes = channels * tile_cols
    return pl.pallas_call(
        deposit_kernel,
        out_shape=jax.ShapeDtypeStruct((tile_rows, lanes), jnp.bfloat16),
        grid=(obs // chunk,),
        in_specs=[
            pl.BlockSpec((chunk, channels), lambda k: (k, 0)),
            pl.BlockSpec((chunk, 1), lambda k: (k, 0)),
            pl.BlockSpec((1, chunk), lambda k: (0, k)),
            pl.BlockSpec((4, chunk), lambda k: (0, k)),
        ],
        out_specs=pl.BlockSpec((tile_rows, lanes), lambda k: (0, 0)),
        scratch_shapes=[
            pltpu.VMEM((2, tile_rows, lanes), jnp.float32),
            pltpu.VMEM((chunk, lanes), jnp.bfloat16),
        ],
        compiler_params=pltpu.CompilerParams(
            dimension_semantics=("arbitrary",), vmem_limit_bytes=48 * 1024 * 1024
        ),
        cost_estimate=pl.CostEstimate(
            flops=4 * tile_rows * lanes * obs, bytes_accessed=obs * 48 + tile_rows * lanes * 2,
            transcendentals=0,
        ),
    )(vals_col, by_col, bx_row, w_row)


def shards(owner_tile, corner_cell, weights, innovations, x_inverse, y_inverse):
    lon_count = lax.axis_size("lon")
    lat_count = lax.axis_size("lat")
    devices = lon_count * lat_count
    channels = innovations.shape[0]
    obs_count = innovations.shape[1]
    line_x = x_inverse.shape[0]
    tile_rows = line_x // lon_count
    line_y = y_inverse.shape[0]
    tile_cols = line_y // lat_count
    capacity = 5 * obs_count // (2 * devices)
    got = route_obs(owner_tile, corner_cell, weights, innovations, devices, capacity, tile_cols)
    increment = deposit(got, channels, tile_rows, tile_cols)
    pair = channels // lon_count
    lanes = pair * tile_cols
    by_pair = increment.reshape(tile_rows, lon_count, lanes).transpose(1, 0, 2)
    lines_x = lax.all_to_all(by_pair, "lon", 0, 0, tiled=True).reshape(line_x, lanes)
    solved_x = jnp.dot(x_inverse, lines_x, preferred_element_type=jnp.float32).astype(jnp.bfloat16)
    stride = tile_rows // lat_count
    by_row = solved_x.reshape(lon_count, stride, lat_count, lanes).transpose(0, 2, 1, 3)
    by_row = by_row.reshape(devices, stride, lanes)
    got = lax.all_to_all(by_row, ("lon", "lat"), 0, 0, tiled=True)
    got = got.reshape(lon_count, lat_count, stride, pair, tile_cols).transpose(0, 3, 2, 1, 4)
    lines_y = got.reshape(channels * stride, line_y)
    solved_y = lax.dot_general(
        lines_y, y_inverse, (((1,), (1,)), ((), ())), preferred_element_type=jnp.float32
    ).astype(jnp.bfloat16)
    solved_y = solved_y.reshape(channels * stride, lat_count, tile_cols)
    tiles = lax.all_to_all(solved_y, "lat", 1, 1, tiled=True)
    return tiles.reshape(channels, tile_rows, tile_cols)


def solution(mesh):
    placed = (
        P(("lon", "lat")),
        P(("lon", "lat")),
        P(None, ("lon", "lat")),
        P(None, ("lon", "lat")),
        P(),
        P(),
    )
    return jax.shard_map(
        shards, mesh=mesh, in_specs=placed, out_specs=P(None, "lon", "lat"), check_vma=False
    )
```

```python
import jax
import jax.numpy as jnp
from jax import lax
from jax.sharding import PartitionSpec as P
from jax.experimental import pallas as pl
from jax.experimental.pallas import tpu as pltpu


def tile_ranks(owner_tile, groups):
    obs_total = owner_tile.shape[0]
    block = 128
    blocks = obs_total // block
    one_hot = (owner_tile[:, None] == jnp.arange(groups, dtype=jnp.int32)[None, :]).astype(
        jnp.bfloat16
    )
    hot_blocks = one_hot.reshape(blocks, block, groups)
    inner = jnp.arange(block, dtype=jnp.int32)
    lower = (inner[None, :] <= inner[:, None]).astype(jnp.bfloat16)
    within = jnp.einsum("ij,bjd->bid", lower, hot_blocks, preferred_element_type=jnp.float32)
    totals = jnp.sum(hot_blocks.astype(jnp.float32), axis=1).astype(jnp.bfloat16)
    outer = jnp.arange(blocks, dtype=jnp.int32)
    before = (outer[None, :] < outer[:, None]).astype(jnp.bfloat16)
    earlier = jnp.dot(before, totals, preferred_element_type=jnp.float32)
    running = (within + earlier[:, None, :]).reshape(obs_total, groups)
    rank = jnp.sum(running * one_hot.astype(jnp.float32), axis=1).astype(jnp.int32) - 1
    return one_hot, rank


def route_obs(owner_tile, corner_cell, weights, innovations, groups, capacity, tile_cols):
    one_hot, rank = tile_ranks(owner_tile, groups)
    cell_x = corner_cell // (tile_cols - 1)
    cell_y = corner_cell % (tile_cols - 1)
    digits = jnp.stack([cell_y, cell_x % 128, cell_x // 128]).astype(jnp.bfloat16)
    stacked = jnp.concatenate([innovations, weights, digits], 0)
    rows = stacked.shape[0]
    rank_hot = rank[None, :] == jnp.arange(capacity, dtype=jnp.int32)[:, None]
    spread = jnp.where(rank_hot[None, :, :], stacked[:, None, :], jnp.zeros((), jnp.bfloat16))
    spread = spread.reshape(rows * capacity, -1)
    send = lax.dot_general(
        one_hot, spread, (((0,), (1,)), ((), ())), preferred_element_type=jnp.float32
    ).astype(jnp.bfloat16)
    got = lax.all_to_all(send, ("lon", "lat"), 0, 0, tiled=True)
    got = got.reshape(groups, rows, capacity).transpose(1, 0, 2).reshape(rows, -1)
    return got


def deposit_kernel(vals_ref, by_ref, bx_ref, w_ref, out_ref, acc_ref, spread_ref):
    step = pl.program_id(0)
    chunk, channels = vals_ref.shape
    tile_rows = out_ref.shape[0]
    tile_cols = out_ref.shape[1] // channels

    @pl.when(step == 0)
    def _():
        acc_ref[...] = jnp.zeros_like(acc_ref)

    zero = jnp.zeros((), jnp.bfloat16)
    lane_y = lax.broadcasted_iota(jnp.int32, (chunk, tile_cols), 1)
    hit_y = lane_y == by_ref[...]
    for c in range(channels):
        spread_ref[:, c * tile_cols : (c + 1) * tile_cols] = jnp.where(
            hit_y, vals_ref[:, c : c + 1], zero
        )
    row_x = lax.broadcasted_iota(jnp.int32, (tile_rows, chunk), 0)
    base_x = bx_ref[...]
    at_x = row_x == base_x
    next_x = row_x == base_x + 1
    for offset_y in range(2):
        near = jnp.where(at_x, w_ref[2 * offset_y : 2 * offset_y + 1, :], zero) + jnp.where(
            next_x, w_ref[2 * offset_y + 1 : 2 * offset_y + 2, :], zero
        )
        acc_ref[offset_y] += jnp.dot(near, spread_ref[...], preferred_element_type=jnp.float32)

    @pl.when(step == pl.num_programs(0) - 1)
    def _():
        later = pltpu.roll(acc_ref[1], 1, 1)
        lane = lax.broadcasted_iota(jnp.int32, later.shape, 1)
        later = jnp.where(lane % tile_cols == 0, 0.0, later)
        out_ref[...] = (acc_ref[0] + later).astype(out_ref.dtype)


def deposit(got, channels, tile_rows, tile_cols):
    obs = got.shape[1]
    chunk = 2560
    vals_col = got[:channels].T
    by_col = got[channels + 4].astype(jnp.int32)[:, None]
    bx_row = (got[channels + 5].astype(jnp.int32) + 128 * got[channels + 6].astype(jnp.int32))[None, :]
    w_row = got[channels : channels + 4]
    lanes = channels * tile_cols
    return pl.pallas_call(
        deposit_kernel,
        out_shape=jax.ShapeDtypeStruct((tile_rows, lanes), jnp.bfloat16),
        grid=(obs // chunk,),
        in_specs=[
            pl.BlockSpec((chunk, channels), lambda k: (k, 0)),
            pl.BlockSpec((chunk, 1), lambda k: (k, 0)),
            pl.BlockSpec((1, chunk), lambda k: (0, k)),
            pl.BlockSpec((4, chunk), lambda k: (0, k)),
        ],
        out_specs=pl.BlockSpec((tile_rows, lanes), lambda k: (0, 0)),
        scratch_shapes=[
            pltpu.VMEM((2, tile_rows, lanes), jnp.float32),
            pltpu.VMEM((chunk, lanes), jnp.bfloat16),
        ],
        compiler_params=pltpu.CompilerParams(
            dimension_semantics=("arbitrary",), vmem_limit_bytes=48 * 1024 * 1024
        ),
        cost_estimate=pl.CostEstimate(
            flops=4 * tile_rows * lanes * obs, bytes_accessed=obs * 48 + tile_rows * lanes * 2,
            transcendentals=0,
        ),
    )(vals_col, by_col, bx_row, w_row)


def shards(owner_tile, corner_cell, weights, innovations, x_inverse, y_inverse):
    lon_count = lax.axis_size("lon")
    lat_count = lax.axis_size("lat")
    devices = lon_count * lat_count
    channels = innovations.shape[0]
    obs_count = innovations.shape[1]
    line_x = x_inverse.shape[0]
    tile_rows = line_x // lon_count
    line_y = y_inverse.shape[0]
    tile_cols = line_y // lat_count
    capacity = 5 * obs_count // (2 * devices)
    got = route_obs(owner_tile, corner_cell, weights, innovations, devices, capacity, tile_cols)
    increment = deposit(got, channels, tile_rows, tile_cols)
    pair = channels // lon_count
    lanes = pair * tile_cols
    by_pair = increment.reshape(tile_rows, lon_count, lanes).transpose(1, 0, 2)
    lines_x = lax.all_to_all(by_pair, "lon", 0, 0, tiled=True).reshape(line_x, lanes)
    solved_x = jnp.dot(x_inverse, lines_x, preferred_element_type=jnp.float32).astype(jnp.bfloat16)
    stride = tile_rows // lat_count
    by_row = solved_x.reshape(lon_count, stride, lat_count, lanes).transpose(0, 2, 1, 3)
    by_row = by_row.reshape(devices, stride, lanes)
    got = lax.all_to_all(by_row, ("lon", "lat"), 0, 0, tiled=True)
    got = got.reshape(lon_count, lat_count, stride, pair, tile_cols).transpose(0, 3, 2, 1, 4)
    lines_y = got.reshape(channels * stride, line_y)
    solved_y = lax.dot_general(
        lines_y, y_inverse, (((1,), (1,)), ((), ())), preferred_element_type=jnp.float32
    ).astype(jnp.bfloat16)
    solved_y = solved_y.reshape(channels * stride, lat_count, tile_cols)
    tiles = lax.all_to_all(solved_y, "lat", 1, 1, tiled=True)
    return tiles.reshape(channels, tile_rows, tile_cols)


def solution(mesh):
    placed = (
        P(("lon", "lat")),
        P(("lon", "lat")),
        P(None, ("lon", "lat")),
        P(None, ("lon", "lat")),
        P(),
        P(),
    )
    return jax.shard_map(
        shards, mesh=mesh, in_specs=placed, out_specs=P(None, "lon", "lat"), check_vma=False
    )
```

```python
import jax
import jax.numpy as jnp
from jax import lax
from jax.sharding import PartitionSpec as P
from jax.experimental import pallas as pl
from jax.experimental.pallas import tpu as pltpu


def tile_ranks(owner_tile, groups):
    obs_total = owner_tile.shape[0]
    block = 128
    blocks = obs_total // block
    one_hot = (owner_tile[:, None] == jnp.arange(groups, dtype=jnp.int32)[None, :]).astype(
        jnp.bfloat16
    )
    hot_blocks = one_hot.reshape(blocks, block, groups)
    inner = jnp.arange(block, dtype=jnp.int32)
    lower = (inner[None, :] <= inner[:, None]).astype(jnp.bfloat16)
    within = jnp.einsum("ij,bjd->bid", lower, hot_blocks, preferred_element_type=jnp.float32)
    totals = jnp.sum(hot_blocks.astype(jnp.float32), axis=1).astype(jnp.bfloat16)
    outer = jnp.arange(blocks, dtype=jnp.int32)
    before = (outer[None, :] < outer[:, None]).astype(jnp.bfloat16)
    earlier = jnp.dot(before, totals, preferred_element_type=jnp.float32)
    running = (within + earlier[:, None, :]).reshape(obs_total, groups)
    rank = jnp.sum(running * one_hot.astype(jnp.float32), axis=1).astype(jnp.int32) - 1
    return one_hot, rank


def route_obs(owner_tile, corner_cell, weights, innovations, groups, capacity, tile_cols):
    one_hot, rank = tile_ranks(owner_tile, groups)
    cell_x = corner_cell // (tile_cols - 1)
    cell_y = corner_cell % (tile_cols - 1)
    digits = jnp.stack([cell_y, cell_x % 128, cell_x // 128]).astype(jnp.bfloat16)
    stacked = jnp.concatenate([innovations, weights, digits], 0)
    rows = stacked.shape[0]
    rank_hot = rank[None, :] == jnp.arange(capacity, dtype=jnp.int32)[:, None]
    spread = jnp.where(rank_hot[None, :, :], stacked[:, None, :], jnp.zeros((), jnp.bfloat16))
    spread = spread.reshape(rows * capacity, -1)
    send = lax.dot_general(
        one_hot, spread, (((0,), (1,)), ((), ())), preferred_element_type=jnp.float32
    ).astype(jnp.bfloat16)
    got = lax.all_to_all(send, ("lon", "lat"), 0, 0, tiled=True)
    got = got.reshape(groups, rows, capacity).transpose(1, 0, 2).reshape(rows, -1)
    return got


def deposit_kernel(vals_ref, by_ref, bx_ref, w_ref, out_ref, acc_ref, spread_ref):
    step = pl.program_id(0)
    channels, chunk = vals_ref.shape
    tile_cols = out_ref.shape[0] // channels
    wide = out_ref.shape[1]

    @pl.when(step == 0)
    def _():
        acc_ref[...] = jnp.zeros_like(acc_ref)

    zero = jnp.zeros((), jnp.bfloat16)
    row_y = lax.broadcasted_iota(jnp.int32, (tile_cols, chunk), 0)
    hit_y = row_y == by_ref[...]
    for c in range(channels):
        spread_ref[c * tile_cols : (c + 1) * tile_cols, :] = jnp.where(
            hit_y, vals_ref[c : c + 1, :], zero
        )
    col_x = lax.broadcasted_iota(jnp.int32, (chunk, wide), 1)
    base_x = bx_ref[...]
    at_x = col_x == base_x
    next_x = col_x == base_x + 1
    for offset_y in range(2):
        near = jnp.where(at_x, w_ref[:, 2 * offset_y : 2 * offset_y + 1], zero) + jnp.where(
            next_x, w_ref[:, 2 * offset_y + 1 : 2 * offset_y + 2], zero
        )
        acc_ref[offset_y] += jnp.dot(spread_ref[...], near, preferred_element_type=jnp.float32)

    @pl.when(step == pl.num_programs(0) - 1)
    def _():
        later = pltpu.roll(acc_ref[1], 1, 0)
        row = lax.broadcasted_iota(jnp.int32, later.shape, 0)
        later = jnp.where(row % tile_cols == 0, 0.0, later)
        out_ref[...] = (acc_ref[0] + later).astype(out_ref.dtype)


def deposit(got, channels, tile_rows, tile_cols):
    obs = got.shape[1]
    chunk = 1280
    wide = -(-tile_rows // 128) * 128
    vals_row = got[:channels]
    by_row = got[channels + 4].astype(jnp.int32)[None, :]
    bx_col = (got[channels + 5].astype(jnp.int32) + 128 * got[channels + 6].astype(jnp.int32))[:, None]
    w_col = got[channels : channels + 4].T
    lanes = channels * tile_cols
    out = pl.pallas_call(
        deposit_kernel,
        out_shape=jax.ShapeDtypeStruct((lanes, wide), jnp.bfloat16),
        grid=(obs // chunk,),
        in_specs=[
            pl.BlockSpec((channels, chunk), lambda k: (0, k)),
            pl.BlockSpec((1, chunk), lambda k: (0, k)),
            pl.BlockSpec((chunk, 1), lambda k: (k, 0)),
            pl.BlockSpec((chunk, 4), lambda k: (k, 0)),
        ],
        out_specs=pl.BlockSpec((lanes, wide), lambda k: (0, 0)),
        scratch_shapes=[
            pltpu.VMEM((2, lanes, wide), jnp.float32),
            pltpu.VMEM((lanes, chunk), jnp.bfloat16),
        ],
        compiler_params=pltpu.CompilerParams(
            dimension_semantics=("arbitrary",), vmem_limit_bytes=48 * 1024 * 1024
        ),
        cost_estimate=pl.CostEstimate(
            flops=4 * wide * lanes * obs, bytes_accessed=obs * 48 + wide * lanes * 2,
            transcendentals=0,
        ),
    )(vals_row, by_row, bx_col, w_col)
    return out[:, :tile_rows].reshape(channels, tile_cols, tile_rows).transpose(0, 2, 1)


def shards(owner_tile, corner_cell, weights, innovations, x_inverse, y_inverse):
    lon_count = lax.axis_size("lon")
    lat_count = lax.axis_size("lat")
    devices = lon_count * lat_count
    channels = innovations.shape[0]
    obs_count = innovations.shape[1]
    line_x = x_inverse.shape[0]
    tile_rows = line_x // lon_count
    line_y = y_inverse.shape[0]
    tile_cols = line_y // lat_count
    capacity = 5 * obs_count // (2 * devices)
    got = route_obs(owner_tile, corner_cell, weights, innovations, devices, capacity, tile_cols)
    increment = deposit(got, channels, tile_rows, tile_cols)
    pair = channels // lon_count
    lanes = pair * tile_cols
    by_pair = increment.reshape(lon_count, pair, tile_rows, tile_cols).transpose(0, 2, 1, 3)
    by_pair = by_pair.reshape(lon_count, tile_rows, lanes)
    lines_x = lax.all_to_all(by_pair, "lon", 0, 0, tiled=True).reshape(line_x, lanes)
    solved_x = jnp.dot(x_inverse, lines_x, preferred_element_type=jnp.float32).astype(jnp.bfloat16)
    stride = tile_rows // lat_count
    by_row = solved_x.reshape(lon_count, stride, lat_count, lanes).transpose(0, 2, 1, 3)
    by_row = by_row.reshape(devices, stride, lanes)
    got = lax.all_to_all(by_row, ("lon", "lat"), 0, 0, tiled=True)
    got = got.reshape(lon_count, lat_count, stride, pair, tile_cols).transpose(0, 3, 2, 1, 4)
    lines_y = got.reshape(channels * stride, line_y)
    solved_y = lax.dot_general(
        lines_y, y_inverse, (((1,), (1,)), ((), ())), preferred_element_type=jnp.float32
    ).astype(jnp.bfloat16)
    solved_y = solved_y.reshape(channels * stride, lat_count, tile_cols)
    tiles = lax.all_to_all(solved_y, "lat", 1, 1, tiled=True)
    return tiles.reshape(channels, tile_rows, tile_cols)


def solution(mesh):
    placed = (
        P(("lon", "lat")),
        P(("lon", "lat")),
        P(None, ("lon", "lat")),
        P(None, ("lon", "lat")),
        P(),
        P(),
    )
    return jax.shard_map(
        shards, mesh=mesh, in_specs=placed, out_specs=P(None, "lon", "lat"), check_vma=False
    )
```

```python
import jax
import jax.numpy as jnp
from jax import lax
from jax.sharding import PartitionSpec as P


def tile_ranks(owner_tile, groups, lon_count, lat_count):
    obs_total = owner_tile.shape[0]
    block = 128
    blocks = obs_total // block
    column = jnp.arange(groups, dtype=jnp.int32)
    tile_of_column = (column % lon_count) * lat_count + column // lon_count
    one_hot = (owner_tile[:, None] == tile_of_column[None, :]).astype(jnp.bfloat16)
    hot_blocks = one_hot.reshape(blocks, block, groups)
    inner = jnp.arange(block, dtype=jnp.int32)
    lower = (inner[None, :] <= inner[:, None]).astype(jnp.bfloat16)
    within = jnp.einsum("ij,bjd->bid", lower, hot_blocks, preferred_element_type=jnp.float32)
    totals = jnp.sum(hot_blocks.astype(jnp.float32), axis=1).astype(jnp.bfloat16)
    outer = jnp.arange(blocks, dtype=jnp.int32)
    before = (outer[None, :] < outer[:, None]).astype(jnp.bfloat16)
    earlier = jnp.dot(before, totals, preferred_element_type=jnp.float32)
    running = (within + earlier[:, None, :]).reshape(obs_total, groups)
    rank = jnp.sum(running * one_hot.astype(jnp.float32), axis=1).astype(jnp.int32) - 1
    return one_hot, rank


def route_obs(owner_tile, corner_cell, weights, innovations, groups, capacity, tile_cols):
    lon_count = lax.axis_size("lon")
    lat_count = lax.axis_size("lat")
    one_hot, rank = tile_ranks(owner_tile, groups, lon_count, lat_count)
    cell_x = corner_cell // (tile_cols - 1)
    cell_y = corner_cell % (tile_cols - 1)
    digits = jnp.stack([cell_y, cell_x % 128, cell_x // 128]).astype(jnp.bfloat16)
    stacked = jnp.concatenate([innovations, weights, digits], 0)
    rows = stacked.shape[0]
    rank_hot = rank[None, :] == jnp.arange(capacity, dtype=jnp.int32)[:, None]
    spread = jnp.where(rank_hot[None, :, :], stacked[:, None, :], jnp.zeros((), jnp.bfloat16))
    spread = spread.reshape(rows * capacity, -1)
    send = lax.dot_general(
        one_hot, spread, (((0,), (1,)), ((), ())), preferred_element_type=jnp.float32
    ).astype(jnp.bfloat16)
    got = lax.all_to_all(send, ("lat", "lon"), 0, 0, tiled=True)
    got = got.reshape(groups, rows, capacity).transpose(1, 0, 2).reshape(rows, -1)
    return got


def deposit(got, channels, tile_rows, tile_cols):
    values = got[:channels]
    got_weights = got[channels : channels + 4]
    base_y = got[channels + 4].astype(jnp.int32)
    base_x = got[channels + 5].astype(jnp.int32) + 128 * got[channels + 6].astype(jnp.int32)
    row_iota = jnp.arange(tile_rows, dtype=jnp.int32)
    col_iota = jnp.arange(tile_cols, dtype=jnp.int32)
    zero_value = jnp.zeros((), jnp.bfloat16)
    raw_total = jnp.zeros((channels, tile_rows, tile_cols), jnp.float32)
    for offset_y in range(2):
        near_rows = jnp.where(
            row_iota[None, :] == base_x[:, None], got_weights[2 * offset_y][:, None], zero_value
        )
        near_rows = near_rows + jnp.where(
            row_iota[None, :] == base_x[:, None] + 1,
            got_weights[2 * offset_y + 1][:, None],
            zero_value,
        )
        spread = jnp.where(
            col_iota[None, :, None] == (base_y + offset_y)[None, None, :],
            values[:, None, :],
            zero_value,
        )
        raw_total = raw_total + jnp.einsum(
            "cyo,ox->cxy", spread, near_rows, preferred_element_type=jnp.float32
        )
    return raw_total.astype(jnp.bfloat16)


def shards(owner_tile, corner_cell, weights, innovations, x_inverse, y_inverse):
    lon_count = lax.axis_size("lon")
    lat_count = lax.axis_size("lat")
    devices = lon_count * lat_count
    channels = innovations.shape[0]
    obs_count = innovations.shape[1]
    line_x = x_inverse.shape[0]
    tile_rows = line_x // lon_count
    line_y = y_inverse.shape[0]
    tile_cols = line_y // lat_count
    capacity = 5 * obs_count // (2 * devices)
    got = route_obs(owner_tile, corner_cell, weights, innovations, devices, capacity, tile_cols)
    increment = deposit(got, channels, tile_rows, tile_cols)
    pair = channels // lon_count
    lanes = pair * tile_cols
    by_pair = increment.reshape(lon_count, pair, tile_rows, tile_cols).transpose(0, 2, 1, 3)
    by_pair = by_pair.reshape(lon_count, tile_rows, lanes)
    lines_x = lax.all_to_all(by_pair, "lon", 0, 0, tiled=True).reshape(line_x, lanes)
    solved_x = jnp.dot(x_inverse, lines_x, preferred_element_type=jnp.float32).astype(jnp.bfloat16)
    stride = tile_rows // lat_count
    by_row = solved_x.reshape(lon_count, stride, lat_count, lanes).transpose(2, 0, 1, 3)
    by_row = by_row.reshape(devices, stride, lanes)
    got = lax.all_to_all(by_row, ("lat", "lon"), 0, 0, tiled=True)
    got = got.reshape(lat_count, lon_count, stride, pair, tile_cols).transpose(1, 3, 2, 0, 4)
    lines_y = got.reshape(channels * stride, line_y)
    solved_y = lax.dot_general(
        lines_y, y_inverse, (((1,), (1,)), ((), ())), preferred_element_type=jnp.float32
    ).astype(jnp.bfloat16)
    solved_y = solved_y.reshape(channels * stride, lat_count, tile_cols)
    tiles = lax.all_to_all(solved_y, "lat", 1, 1, tiled=True)
    return tiles.reshape(channels, tile_rows, tile_cols)


def solution(mesh):
    placed = (
        P(("lon", "lat")),
        P(("lon", "lat")),
        P(None, ("lon", "lat")),
        P(None, ("lon", "lat")),
        P(),
        P(),
    )
    return jax.shard_map(
        shards, mesh=mesh, in_specs=placed, out_specs=P(None, "lon", "lat"), check_vma=False
    )
```

```python
import jax
import jax.numpy as jnp
from jax import lax
from jax.sharding import PartitionSpec as P


def tile_ranks(owner_tile, groups):
    obs_total = owner_tile.shape[0]
    block = 128
    blocks = obs_total // block
    one_hot = (owner_tile[:, None] == jnp.arange(groups, dtype=jnp.int32)[None, :]).astype(
        jnp.bfloat16
    )
    hot_blocks = one_hot.reshape(blocks, block, groups)
    inner = jnp.arange(block, dtype=jnp.int32)
    lower = (inner[None, :] <= inner[:, None]).astype(jnp.bfloat16)
    within = jnp.einsum("ij,bjd->bid", lower, hot_blocks, preferred_element_type=jnp.float32)
    totals = jnp.sum(hot_blocks.astype(jnp.float32), axis=1).astype(jnp.bfloat16)
    outer = jnp.arange(blocks, dtype=jnp.int32)
    before = (outer[None, :] < outer[:, None]).astype(jnp.bfloat16)
    earlier = jnp.dot(before, totals, preferred_element_type=jnp.float32)
    running = (within + earlier[:, None, :]).reshape(obs_total, groups)
    rank = jnp.sum(running * one_hot.astype(jnp.float32), axis=1).astype(jnp.int32) - 1
    return one_hot, rank


def route_obs(owner_tile, corner_cell, weights, innovations, groups, capacity, tile_cols):
    one_hot, rank = tile_ranks(owner_tile, groups)
    cell_x = corner_cell // (tile_cols - 1)
    cell_y = corner_cell % (tile_cols - 1)
    digits = jnp.stack([cell_y, cell_x % 128, cell_x // 128]).astype(jnp.bfloat16)
    stacked = jnp.concatenate([innovations, weights, digits], 0)
    rows = stacked.shape[0]
    rank_hot = rank[None, :] == jnp.arange(capacity, dtype=jnp.int32)[:, None]
    spread = jnp.where(rank_hot[None, :, :], stacked[:, None, :], jnp.zeros((), jnp.bfloat16))
    spread = spread.reshape(rows * capacity, -1)
    send = lax.dot_general(
        one_hot, spread, (((0,), (1,)), ((), ())), preferred_element_type=jnp.float32
    ).astype(jnp.bfloat16)
    got = lax.all_to_all(send, ("lon", "lat"), 0, 0, tiled=True)
    got = got.reshape(groups, rows, capacity).transpose(1, 0, 2).reshape(rows, -1)
    return got


def deposit(got, channels, tile_rows, tile_cols):
    values = got[:channels]
    got_weights = got[channels : channels + 4]
    base_y = got[channels + 4].astype(jnp.int32)
    base_x = got[channels + 5].astype(jnp.int32) + 128 * got[channels + 6].astype(jnp.int32)
    row_iota = jnp.arange(tile_rows, dtype=jnp.int32)
    col_iota = jnp.arange(tile_cols, dtype=jnp.int32)
    zero_value = jnp.zeros((), jnp.bfloat16)
    raw_total = jnp.zeros((channels, tile_rows, tile_cols), jnp.float32)
    for offset_y in range(2):
        near_rows = jnp.where(
            row_iota[None, :] == base_x[:, None], got_weights[2 * offset_y][:, None], zero_value
        )
        near_rows = near_rows + jnp.where(
            row_iota[None, :] == base_x[:, None] + 1,
            got_weights[2 * offset_y + 1][:, None],
            zero_value,
        )
        spread = jnp.where(
            col_iota[None, :, None] == (base_y + offset_y)[None, None, :],
            values[:, None, :],
            zero_value,
        )
        raw_total = raw_total + jnp.einsum(
            "cyo,ox->cxy", spread, near_rows, preferred_element_type=jnp.float32
        )
    return raw_total.astype(jnp.bfloat16)


def shards(owner_tile, corner_cell, weights, innovations, x_inverse, y_inverse):
    lon_count = lax.axis_size("lon")
    lat_count = lax.axis_size("lat")
    devices = lon_count * lat_count
    channels = innovations.shape[0]
    obs_count = innovations.shape[1]
    line_x = x_inverse.shape[0]
    tile_rows = line_x // lon_count
    line_y = y_inverse.shape[0]
    tile_cols = line_y // lat_count
    capacity = 5 * obs_count // (2 * devices)
    got = route_obs(owner_tile, corner_cell, weights, innovations, devices, capacity, tile_cols)
    increment = deposit(got, channels, tile_rows, tile_cols)
    pair = channels // lon_count
    lanes = pair * tile_cols
    by_pair = increment.reshape(lon_count, pair, tile_rows, tile_cols).transpose(0, 2, 1, 3)
    by_pair = by_pair.reshape(lon_count, tile_rows, lanes)
    lines_x = lax.all_to_all(by_pair, "lon", 0, 0, tiled=True).reshape(line_x, lanes)
    solved_x = jnp.dot(x_inverse, lines_x, preferred_element_type=jnp.float32).astype(jnp.bfloat16)
    stride = tile_rows // lat_count
    by_row = solved_x.reshape(lon_count, stride, lat_count, pair, tile_cols).transpose(0, 2, 1, 3, 4)
    by_row = by_row.reshape(devices, stride * pair, tile_cols)
    got = lax.all_to_all(by_row, ("lon", "lat"), 0, 0, tiled=True)
    got = got.reshape(lon_count, lat_count, stride, pair, tile_cols).transpose(0, 3, 2, 1, 4)
    lines_y = got.reshape(channels * stride, line_y)
    solved_y = lax.dot_general(
        lines_y, y_inverse, (((1,), (1,)), ((), ())), preferred_element_type=jnp.float32
    ).astype(jnp.bfloat16)
    solved_y = solved_y.reshape(channels * stride, lat_count, tile_cols)
    tiles = lax.all_to_all(solved_y, "lat", 1, 1, tiled=True)
    return tiles.reshape(channels, tile_rows, tile_cols)


def solution(mesh):
    placed = (
        P(("lon", "lat")),
        P(("lon", "lat")),
        P(None, ("lon", "lat")),
        P(None, ("lon", "lat")),
        P(),
        P(),
    )
    return jax.shard_map(
        shards, mesh=mesh, in_specs=placed, out_specs=P(None, "lon", "lat"), check_vma=False
    )
```

```python
import jax
import jax.numpy as jnp
from jax import lax
from jax.sharding import PartitionSpec as P


def tile_ranks(owner_tile, groups):
    obs_total = owner_tile.shape[0]
    block = 128
    blocks = obs_total // block
    one_hot = (owner_tile[:, None] == jnp.arange(groups, dtype=jnp.int32)[None, :]).astype(
        jnp.bfloat16
    )
    hot_blocks = one_hot.reshape(blocks, block, groups)
    inner = jnp.arange(block, dtype=jnp.int32)
    lower = (inner[None, :] <= inner[:, None]).astype(jnp.bfloat16)
    within = jnp.einsum("ij,bjd->bid", lower, hot_blocks, preferred_element_type=jnp.float32)
    totals = jnp.sum(hot_blocks.astype(jnp.float32), axis=1).astype(jnp.bfloat16)
    outer = jnp.arange(blocks, dtype=jnp.int32)
    before = (outer[None, :] < outer[:, None]).astype(jnp.bfloat16)
    earlier = jnp.dot(before, totals, preferred_element_type=jnp.float32)
    running = (within + earlier[:, None, :]).reshape(obs_total, groups)
    rank = jnp.sum(running * one_hot.astype(jnp.float32), axis=1).astype(jnp.int32) - 1
    return one_hot, rank


def route_obs(owner_tile, corner_cell, weights, innovations, groups, capacity, tile_cols):
    one_hot, rank = tile_ranks(owner_tile, groups)
    cell_x = corner_cell // (tile_cols - 1)
    cell_y = corner_cell % (tile_cols - 1)
    digits = jnp.stack([cell_y, cell_x % 128, cell_x // 128]).astype(jnp.bfloat16)
    stacked = jnp.concatenate([innovations, weights, digits], 0)
    rows = stacked.shape[0]
    rank_hot = rank[None, :] == jnp.arange(capacity, dtype=jnp.int32)[:, None]
    spread = jnp.where(rank_hot[None, :, :], stacked[:, None, :], jnp.zeros((), jnp.bfloat16))
    spread = spread.reshape(rows * capacity, -1)
    send = lax.dot_general(
        one_hot, spread, (((0,), (1,)), ((), ())), preferred_element_type=jnp.float32
    ).astype(jnp.bfloat16)
    message = send.shape[1]
    padded = -(-message // 1024) * 1024
    send = jnp.pad(send, ((0, 0), (0, padded - message)))
    got = lax.all_to_all(send, ("lon", "lat"), 0, 0, tiled=True)[:, :message]
    got = got.reshape(groups, rows, capacity).transpose(1, 0, 2).reshape(rows, -1)
    return got


def deposit(got, channels, tile_rows, tile_cols):
    values = got[:channels]
    got_weights = got[channels : channels + 4]
    base_y = got[channels + 4].astype(jnp.int32)
    base_x = got[channels + 5].astype(jnp.int32) + 128 * got[channels + 6].astype(jnp.int32)
    row_iota = jnp.arange(tile_rows, dtype=jnp.int32)
    col_iota = jnp.arange(tile_cols, dtype=jnp.int32)
    zero_value = jnp.zeros((), jnp.bfloat16)
    raw_total = jnp.zeros((channels, tile_rows, tile_cols), jnp.float32)
    for offset_y in range(2):
        near_rows = jnp.where(
            row_iota[None, :] == base_x[:, None], got_weights[2 * offset_y][:, None], zero_value
        )
        near_rows = near_rows + jnp.where(
            row_iota[None, :] == base_x[:, None] + 1,
            got_weights[2 * offset_y + 1][:, None],
            zero_value,
        )
        spread = jnp.where(
            col_iota[None, :, None] == (base_y + offset_y)[None, None, :],
            values[:, None, :],
            zero_value,
        )
        raw_total = raw_total + jnp.einsum(
            "cyo,ox->cxy", spread, near_rows, preferred_element_type=jnp.float32
        )
    return raw_total.astype(jnp.bfloat16)


def shards(owner_tile, corner_cell, weights, innovations, x_inverse, y_inverse):
    lon_count = lax.axis_size("lon")
    lat_count = lax.axis_size("lat")
    devices = lon_count * lat_count
    channels = innovations.shape[0]
    obs_count = innovations.shape[1]
    line_x = x_inverse.shape[0]
    tile_rows = line_x // lon_count
    line_y = y_inverse.shape[0]
    tile_cols = line_y // lat_count
    capacity = 5 * obs_count // (2 * devices)
    got = route_obs(owner_tile, corner_cell, weights, innovations, devices, capacity, tile_cols)
    increment = deposit(got, channels, tile_rows, tile_cols)
    pair = channels // lon_count
    lanes = pair * tile_cols
    by_pair = increment.reshape(lon_count, pair, tile_rows, tile_cols).transpose(0, 2, 1, 3)
    by_pair = by_pair.reshape(lon_count, tile_rows, lanes)
    lines_x = lax.all_to_all(by_pair, "lon", 0, 0, tiled=True).reshape(line_x, lanes)
    solved_x = jnp.dot(x_inverse, lines_x, preferred_element_type=jnp.float32).astype(jnp.bfloat16)
    stride = tile_rows // lat_count
    by_row = solved_x.reshape(lon_count, stride, lat_count, pair, tile_cols).transpose(0, 2, 1, 3, 4)
    by_row = by_row.reshape(devices, stride * pair, tile_cols)
    got = lax.all_to_all(by_row, ("lon", "lat"), 0, 0, tiled=True)
    got = got.reshape(lon_count, lat_count, stride, pair, tile_cols).transpose(0, 3, 2, 1, 4)
    lines_y = got.reshape(channels * stride, line_y)
    solved_y = lax.dot_general(
        lines_y, y_inverse, (((1,), (1,)), ((), ())), preferred_element_type=jnp.float32
    ).astype(jnp.bfloat16)
    solved_y = solved_y.reshape(channels * stride, lat_count, tile_cols)
    tiles = lax.all_to_all(solved_y, "lat", 1, 1, tiled=True)
    return tiles.reshape(channels, tile_rows, tile_cols)


def solution(mesh):
    placed = (
        P(("lon", "lat")),
        P(("lon", "lat")),
        P(None, ("lon", "lat")),
        P(None, ("lon", "lat")),
        P(),
        P(),
    )
    return jax.shard_map(
        shards, mesh=mesh, in_specs=placed, out_specs=P(None, "lon", "lat"), check_vma=False
    )
```

```python
import jax
import jax.numpy as jnp
from jax import lax
from jax.sharding import PartitionSpec as P


def tile_ranks(owner_tile, groups):
    obs_total = owner_tile.shape[0]
    block = 128
    blocks = obs_total // block
    one_hot = (owner_tile[:, None] == jnp.arange(groups, dtype=jnp.int32)[None, :]).astype(
        jnp.bfloat16
    )
    hot_blocks = one_hot.reshape(blocks, block, groups)
    inner = jnp.arange(block, dtype=jnp.int32)
    lower = (inner[None, :] <= inner[:, None]).astype(jnp.bfloat16)
    within = jnp.einsum("ij,bjd->bid", lower, hot_blocks, preferred_element_type=jnp.float32)
    totals = jnp.sum(hot_blocks.astype(jnp.float32), axis=1).astype(jnp.bfloat16)
    outer = jnp.arange(blocks, dtype=jnp.int32)
    before = (outer[None, :] < outer[:, None]).astype(jnp.bfloat16)
    earlier = jnp.dot(before, totals, preferred_element_type=jnp.float32)
    running = (within + earlier[:, None, :]).reshape(obs_total, groups)
    rank = jnp.sum(running * one_hot.astype(jnp.float32), axis=1).astype(jnp.int32) - 1
    return one_hot, rank


def route_obs(owner_tile, corner_cell, weights, innovations, groups, capacity, tile_cols):
    one_hot, rank = tile_ranks(owner_tile, groups)
    cell_x = corner_cell // (tile_cols - 1)
    cell_y = corner_cell % (tile_cols - 1)
    digits = jnp.stack([cell_y, cell_x % 128, cell_x // 128]).astype(jnp.bfloat16)
    stacked = jnp.concatenate([innovations, weights, digits], 0)
    rows = stacked.shape[0]
    rank_hot = rank[None, :] == jnp.arange(capacity, dtype=jnp.int32)[:, None]
    spread = jnp.where(rank_hot[None, :, :], stacked[:, None, :], jnp.zeros((), jnp.bfloat16))
    spread = spread.reshape(rows * capacity, -1)
    send = lax.dot_general(
        one_hot, spread, (((0,), (1,)), ((), ())), preferred_element_type=jnp.float32
    ).astype(jnp.bfloat16)
    got = lax.all_to_all(send, ("lon", "lat"), 0, 0, tiled=True)
    got = got.reshape(groups, rows, capacity).transpose(1, 0, 2).reshape(rows, -1)
    return got


def deposit(got, channels, tile_rows, tile_cols):
    values = got[:channels]
    got_weights = got[channels : channels + 4]
    base_y = got[channels + 4].astype(jnp.int32)
    base_x = got[channels + 5].astype(jnp.int32) + 128 * got[channels + 6].astype(jnp.int32)
    row_iota = jnp.arange(tile_rows, dtype=jnp.int32)
    col_iota = jnp.arange(tile_cols, dtype=jnp.int32)
    zero_value = jnp.zeros((), jnp.bfloat16)
    raw_total = None
    for offset_y in range(2):
        near_rows = jnp.where(
            row_iota[None, :] == base_x[:, None], got_weights[2 * offset_y][:, None], zero_value
        )
        near_rows = near_rows + jnp.where(
            row_iota[None, :] == base_x[:, None] + 1,
            got_weights[2 * offset_y + 1][:, None],
            zero_value,
        )
        spread = jnp.where(
            col_iota[None, :, None] == (base_y + offset_y)[None, None, :],
            values[:, None, :],
            zero_value,
        )
        part = jnp.einsum("cyo,ox->cxy", spread, near_rows, preferred_element_type=jnp.float32)
        raw_total = part.astype(jnp.bfloat16) if raw_total is None else part + raw_total
    return raw_total.astype(jnp.bfloat16)


def shards(owner_tile, corner_cell, weights, innovations, x_inverse, y_inverse):
    lon_count = lax.axis_size("lon")
    lat_count = lax.axis_size("lat")
    devices = lon_count * lat_count
    channels = innovations.shape[0]
    obs_count = innovations.shape[1]
    line_x = x_inverse.shape[0]
    tile_rows = line_x // lon_count
    line_y = y_inverse.shape[0]
    tile_cols = line_y // lat_count
    capacity = 5 * obs_count // (2 * devices)
    got = route_obs(owner_tile, corner_cell, weights, innovations, devices, capacity, tile_cols)
    increment = deposit(got, channels, tile_rows, tile_cols)
    pair = channels // lon_count
    lanes = pair * tile_cols
    by_pair = increment.reshape(lon_count, pair, tile_rows, tile_cols).transpose(0, 2, 1, 3)
    by_pair = by_pair.reshape(lon_count, tile_rows, lanes)
    lines_x = lax.all_to_all(by_pair, "lon", 0, 0, tiled=True).reshape(line_x, lanes)
    solved_x = jnp.dot(x_inverse, lines_x, preferred_element_type=jnp.float32).astype(jnp.bfloat16)
    stride = tile_rows // lat_count
    by_row = solved_x.reshape(lon_count, stride, lat_count, pair, tile_cols).transpose(0, 2, 1, 3, 4)
    by_row = by_row.reshape(devices, stride * pair, tile_cols)
    got = lax.all_to_all(by_row, ("lon", "lat"), 0, 0, tiled=True)
    got = got.reshape(lon_count, lat_count, stride, pair, tile_cols).transpose(0, 3, 2, 1, 4)
    lines_y = got.reshape(channels * stride, line_y)
    solved_y = lax.dot_general(
        lines_y, y_inverse, (((1,), (1,)), ((), ())), preferred_element_type=jnp.float32
    ).astype(jnp.bfloat16)
    solved_y = solved_y.reshape(channels * stride, lat_count, tile_cols)
    tiles = lax.all_to_all(solved_y, "lat", 1, 1, tiled=True)
    return tiles.reshape(channels, tile_rows, tile_cols)


def solution(mesh):
    placed = (
        P(("lon", "lat")),
        P(("lon", "lat")),
        P(None, ("lon", "lat")),
        P(None, ("lon", "lat")),
        P(),
        P(),
    )
    return jax.shard_map(
        shards, mesh=mesh, in_specs=placed, out_specs=P(None, "lon", "lat"), check_vma=False
    )
```
